256 devices in a mesh: dp: 64 (over x, z, core), pipe: 4 (over y).
Axes of the slice: x: 4, y: 4, z: 8, core: 2. Of those that a mesh axis runs over, the one named last changes fastest.
Arguments:
- tokens: bfloat16 [8192, 2560], P('dp'), may hold values from -6 to 6
- norm_gains: bfloat16 [4, 2560], P('pipe', 'dp'), may hold values from 0.099609375 to 1.8984375
- up_weights: bfloat16 [4, 64, 128, 128], P('pipe', 'dp'), may hold values from -0.5 to 0.5
- down_weights: bfloat16 [4, 64, 128, 128], P('pipe', 'dp'), may hold values from -0.3125 to 0.3125
- coords: int32 [4, 4, 64], P('pipe'), may hold values from 0 to 79, as said below
- cotangent: bfloat16 [8192, 2560], P('dp'), may hold values from -6 to 6
Outputs:
- grad_up: float32 [4, 64, 128, 128], P('pipe', 'dp')
- grad_down: float32 [4, 64, 128, 128], P('pipe', 'dp')
- grad_gain: float32 [4, 2560], P('pipe', 'dp')
- grad_inputs: bfloat16 [4, 8192, 2560], P('pipe', 'dp')
The draws below stay inside these ranges and needn't reach their ends.
Inputs may be any that keep to these rules, and one draw needn't show every extreme that they name: For every layer the 64 pairs (coords[l,0,b], coords[l,1,b]) are distinct, and so are the pairs (coords[l,2,b], coords[l,3,b]); rows 0 and 3 lie below 20, rows 1 and 2 below 80.
All inputs are finite; a program needn't handle non-finite values.
Results may differ from the reference program's by a relative error of at most 0.011.
Values may be sent and summed in bfloat16 or wider, within the bound.
No kernel may reach another device: no remote copies, remote signals or barrier semaphores. Data moves between devices by JAX's collectives and lax.ppermute only.
A program may use at most 128 MiB of HBM per device.

```python
import math
import jax
import jax.numpy as jnp
from jax import lax

D = 2560
FF = 10240
BLOCK = 128
NB = 64
TOK_DEV = 128
LAYERS = 4
TOKENS = 8192
N_DP = 64


def chosen_pairs(key, total_pairs):
    middle = jax.random.permutation(key, total_pairs - 2)[:NB - 2] + 1
    ends = jnp.array([0, total_pairs - 1], dtype=jnp.int32)
    joined = jnp.concatenate([ends, middle.astype(jnp.int32)])
    shuffle = jax.random.permutation(jax.random.fold_in(key, 7), NB)
    return joined[shuffle]


def draw_coords(key, part):
    model_panels = D // BLOCK
    hidden_panels = FF // BLOCK
    total_pairs = model_panels * hidden_panels
    layer_list = []
    for layer_index in range(LAYERS):
        up_order = chosen_pairs(jax.random.fold_in(key, 2 * layer_index + 11), total_pairs)
        down_order = chosen_pairs(jax.random.fold_in(key, 2 * layer_index + 12), total_pairs)
        layer_list.append(jnp.stack([up_order // hidden_panels, up_order % hidden_panels, down_order // model_panels, down_order % model_panels]))
    return jnp.stack(layer_list).astype(jnp.int32)


def levels(stream_key, shape, pieces, smallest, largest):
    factor_of, own = 1.0, jax.random.fold_in(stream_key, 6)
    for dim, shards_of in pieces:
        draws = jnp.exp(jax.random.uniform(jax.random.fold_in(own, dim), (shards_of,), jnp.float32, smallest / len(pieces), largest / len(pieces)))
        factor_of = factor_of * jnp.repeat(draws, shape[dim] // shards_of).reshape([-1 if axis == dim else 1 for axis in range(len(shape))])
    return factor_of


def normal_values(rng, extent, width, most, shards=(), kind=jnp.bfloat16):
    values = jax.random.normal(rng, extent, jnp.float32) * width
    if len(shards) > 0:
        values = levels(rng, extent, shards, -0.22, 0.18) * values
    return jnp.clip(values, min=-most, max=most).astype(kind)


def setup_inputs(seed: int = 0) -> dict:
    key_of = jax.random.split(jax.random.key(seed), 7)
    return {
        "tokens": normal_values(key_of[0], (TOKENS, D), 1.0, 6.0, ((0, 64),)),
        "norm_gains": jnp.clip(1.0 + 0.18 * jax.random.normal(key_of[1], (LAYERS, D), jnp.float32), 0.099609375, 1.8984375).astype(jnp.bfloat16),
        "up_weights": normal_values(key_of[2], (LAYERS, NB, BLOCK, BLOCK), (BLOCK * max(1, NB * BLOCK // FF)) ** -0.5, 0.5, ((0, 4), (1, 64))),
        "down_weights": normal_values(key_of[3], (LAYERS, NB, BLOCK, BLOCK), (BLOCK * max(1, NB * BLOCK // D)) ** -0.5, 0.3125, ((0, 4), (1, 64))),
        "coords": draw_coords(jax.random.fold_in(key_of[6], 71), 0),
        "cotangent": normal_values(key_of[5], (TOKENS, D), 1.0, 6.0, ((0, 64),)),
    }


epsilon = 1e-05

def rounded(values):
    return lax.optimization_barrier(values.astype(jnp.bfloat16))

def norm_parts(inputs, gain_row):
    widened = inputs.astype(jnp.float32)
    inverse = lax.rsqrt(lax.optimization_barrier(jnp.mean(widened * widened, axis=-1, keepdims=True)) + epsilon)
    unit_rows = widened * inverse
    normed = rounded(unit_rows * gain_row.astype(jnp.float32))
    return (widened, inverse, unit_rows, normed)

def pick_panels(values, indices):
    row_count = values.shape[0]
    return jnp.take(values.reshape(row_count, -1, BLOCK), indices, axis=0 + 1).astype(jnp.float32)

def block_product(values, blocks, pick_index, put_index, put_panels, form):
    picked = pick_panels(values, pick_index)
    products = jnp.einsum(form, picked, blocks.astype(jnp.float32), precision=lax.Precision.HIGHEST)
    summed = jax.ops.segment_sum(products, put_index, num_segments=put_panels)
    return jnp.transpose(summed, (1, 0, 2)).reshape(values.shape[0], put_panels * BLOCK)

def block_grads(inputs, outgoing, in_index, out_index):
    return jnp.einsum('rbi,rbo->bio', pick_panels(inputs, in_index), pick_panels(outgoing, out_index), precision=lax.Precision.HIGHEST)

def layer_forward(inputs, gain_row, up_blocks, down_blocks, block_links):
    widened, inverse, unit_rows, normed = norm_parts(inputs, gain_row)
    before = block_product(normed, up_blocks, block_links[0], block_links[1], FF // BLOCK, 'rbi,bio->bro')
    active = rounded(jax.nn.gelu(before))
    added = block_product(active, down_blocks, block_links[2], block_links[3], D // BLOCK, 'rbi,bio->bro')
    return (widened + added).astype(jnp.bfloat16)

def layer_backward(inputs, upstream, gain_row, up_blocks, down_blocks, block_links):
    widened, inverse, unit_rows, normed = norm_parts(inputs, gain_row)
    before = block_product(normed, up_blocks, block_links[0], block_links[1], FF // BLOCK, 'rbi,bio->bro')
    active = rounded(jax.nn.gelu(before))
    grad_active = block_product(upstream, down_blocks, block_links[3], block_links[2], FF // BLOCK, 'rbo,bio->bri')
    down_grad = block_grads(active, upstream, block_links[2], block_links[3])
    gelu_slope = jax.jvp(jax.nn.gelu, (before,), (jnp.ones_like(before),))[1]
    grad_before = rounded(grad_active * gelu_slope)
    grad_normed = block_product(grad_before, up_blocks, block_links[1], block_links[0], D // BLOCK, 'rbo,bio->bri')
    up_grad = block_grads(normed, grad_before, block_links[0], block_links[1])
    gain_grad = lax.optimization_barrier(jnp.sum(grad_normed * unit_rows, axis=0))
    grad_unit = grad_normed * gain_row.astype(jnp.float32)
    centered = grad_unit - unit_rows * lax.optimization_barrier(jnp.mean(grad_unit * unit_rows, axis=-1, keepdims=True))
    grad_local = (upstream.astype(jnp.float32) + inverse * centered).astype(jnp.bfloat16)
    return (grad_local, up_grad, down_grad, gain_grad)

def reference(tokens, norm_gains, up_weights, down_weights, coords, cotangent):
    layer_inputs = []
    current = tokens
    for layer_index in range(LAYERS):
        layer_inputs.append(current)
        gain_row = norm_gains[layer_index]
        up_blocks = up_weights[layer_index]
        down_blocks = down_weights[layer_index]
        block_links = coords[layer_index]

        def forward_rows(row_group, gain_row=gain_row, up_blocks=up_blocks, down_blocks=down_blocks, block_links=block_links):
            return layer_forward(row_group, gain_row, up_blocks, down_blocks, block_links)
        current = lax.map(forward_rows, current.reshape(N_DP, TOK_DEV, D)).reshape(TOKENS, D)
    grad_scale = 1.0 / math.sqrt(TOKENS)
    upstream = cotangent
    ups = [None] * LAYERS
    downs = [None] * LAYERS
    gain_list = [None] * LAYERS
    input_list = [None] * LAYERS
    for layer_index in reversed(range(LAYERS)):
        gain_row = norm_gains[layer_index]
        up_blocks = up_weights[layer_index]
        down_blocks = down_weights[layer_index]
        block_links = coords[layer_index]

        def backward_rows(carried, row_pair, gain_row=gain_row, up_blocks=up_blocks, down_blocks=down_blocks, block_links=block_links):
            result = layer_backward(row_pair[0], row_pair[1], gain_row, up_blocks, down_blocks, block_links)
            return ((carried[0] + result[1], carried[1] + result[2], carried[2] + result[3]), result[0])
        initial = (jnp.zeros((NB, BLOCK, BLOCK), jnp.float32), jnp.zeros((NB, BLOCK, BLOCK), jnp.float32), jnp.zeros((D,), jnp.float32))
        totals, grad_rows = lax.scan(backward_rows, initial, (layer_inputs[layer_index].reshape(N_DP, TOK_DEV, D), upstream.reshape(N_DP, TOK_DEV, D)))
        upstream = grad_rows.reshape(TOKENS, D)
        ups[layer_index] = totals[0] * grad_scale
        downs[layer_index] = totals[1] * grad_scale
        gain_list[layer_index] = totals[2] * grad_scale
        input_list[layer_index] = upstream
    return (jnp.stack(ups), jnp.stack(downs), jnp.stack(gain_list), jnp.stack(input_list))
```

```python
import math

import jax
import jax.numpy as jnp
from jax import lax
from jax.sharding import PartitionSpec as P

FF = 10240
MICRO = 2


epsilon = 1e-05


def from_behind(value, axis, by):
    size = lax.axis_size(axis)
    pairs = [(i, i + by) for i in range(size) if 0 <= i + by < size]
    return lax.ppermute(value, axis, pairs)


def norm_parts(inputs, gain_row):
    widened = inputs.astype(jnp.float32)
    inverse = lax.rsqrt(jnp.mean(widened * widened, axis=-1, keepdims=True) + epsilon)
    unit_rows = widened * inverse
    normed = (unit_rows * gain_row.astype(jnp.float32)).astype(jnp.bfloat16)
    return (widened, inverse, unit_rows, normed)


def to_panels(values, panel_width):
    row_count = values.shape[0]
    return jnp.transpose(values.reshape(row_count, -1, panel_width), (1, 0, 2))


def from_panels(panels):
    return jnp.transpose(panels, (1, 0, 2)).reshape(
        panels.shape[1], panels.shape[0] * panels.shape[2]
    )


def panel_product(panels, blocks, pick_index, put_index, put_count, form):
    picked = jnp.take(panels, pick_index, axis=0)
    products = jnp.einsum(form, picked, blocks, preferred_element_type=jnp.float32)
    placing = (put_index[:, None] == jnp.arange(put_count, dtype=jnp.int32)[None, :]).astype(
        jnp.float32
    )
    return jnp.einsum("brc,bp->prc", products, placing, precision=lax.Precision.HIGHEST)


def up_product(inputs, gain_row, up_blocks, block_links, hidden_panels, panel_width):
    normed = norm_parts(inputs, gain_row)[3]
    return panel_product(
        to_panels(normed, panel_width),
        up_blocks,
        block_links[0],
        block_links[1],
        hidden_panels,
        "bri,bio->bro",
    )


def layer_forward(
    inputs, gain_row, up_blocks, down_blocks, block_links, hidden_panels, model_panels, panel_width
):
    widened, inverse, unit_rows, normed = norm_parts(inputs, gain_row)
    before = panel_product(
        to_panels(normed, panel_width),
        up_blocks,
        block_links[0],
        block_links[1],
        hidden_panels,
        "bri,bio->bro",
    )
    active = jax.nn.gelu(before).astype(jnp.bfloat16)
    added = from_panels(
        panel_product(
            active, down_blocks, block_links[2], block_links[3], model_panels, "bri,bio->bro"
        )
    )
    return ((widened + added).astype(jnp.bfloat16), before)


def layer_backward(
    inputs,
    upstream,
    before,
    gain_row,
    up_blocks,
    down_blocks,
    block_links,
    hidden_panels,
    model_panels,
    panel_width,
):
    widened, inverse, unit_rows, normed = norm_parts(inputs, gain_row)
    upstream_panels = to_panels(upstream, panel_width)
    active_full, gelu_slope = jax.jvp(jax.nn.gelu, (before,), (jnp.ones_like(before),))
    active = active_full.astype(jnp.bfloat16)
    grad_active = panel_product(
        upstream_panels, down_blocks, block_links[3], block_links[2], hidden_panels, "bro,bio->bri"
    )
    grad_before = (grad_active * gelu_slope).astype(jnp.bfloat16)
    grad_normed = from_panels(
        panel_product(
            grad_before, up_blocks, block_links[1], block_links[0], model_panels, "bro,bio->bri"
        )
    )
    gain_grad = jnp.sum(grad_normed * unit_rows, axis=0)
    grad_unit = grad_normed * gain_row.astype(jnp.float32)
    centered = grad_unit - unit_rows * jnp.mean(grad_unit * unit_rows, axis=-1, keepdims=True)
    grad_local = (upstream.astype(jnp.float32) + inverse * centered).astype(jnp.bfloat16)
    return (
        grad_local,
        gain_grad,
        to_panels(normed, panel_width),
        active,
        grad_before,
        upstream_panels,
    )


def own_slots(collected, first):
    stacked = jnp.stack(collected)
    return lax.dynamic_slice_in_dim(stacked, first, MICRO, 0)


def shards(tokens, norm_gains, up_weights, down_weights, coords, cotangent):
    phases = lax.axis_size("pipe")
    section = lax.axis_index("pipe")
    panel_width = up_weights.shape[2]
    model_width = tokens.shape[1]
    token_rows = tokens.shape[0]
    hidden_panels = FF // panel_width
    model_panels = model_width // panel_width
    group_rows = token_rows // MICRO
    block_links = coords[0]
    block_width = panel_width * panel_width
    gain_count = norm_gains.shape[1]
    gain_room = -(-gain_count // 128) * 128
    packed = jnp.concatenate(
        [
            up_weights.reshape(1, 1, block_width),
            down_weights.reshape(1, 1, block_width),
            jnp.pad(norm_gains.reshape(1, 1, gain_count), ((0, 0), (0, 0), (0, gain_room - gain_count))),
        ],
        axis=2,
    )
    gathered = lax.all_gather(packed, "dp", axis=1, tiled=True)[0]
    block_count = gathered.shape[0]
    up_blocks = gathered[:, :block_width].reshape(block_count, panel_width, panel_width)
    down_blocks = gathered[:, block_width : 2 * block_width].reshape(
        block_count, panel_width, panel_width
    )
    gain_row = gathered[:, 2 * block_width : 2 * block_width + gain_count].reshape(-1)
    token_groups = tokens.reshape(MICRO, group_rows, model_width)
    cot_groups = cot_groups_of = cotangent.reshape(MICRO, group_rows, model_width)
    last_tick = MICRO + phases - 2
    input_list = []
    arriving = jnp.zeros((group_rows, model_width), jnp.bfloat16)
    for moment in range(last_tick + 1):
        current = jnp.where(section == 0, token_groups[min(moment, MICRO - 1)], arriving)
        input_list.append(current)
        leaving, before = layer_forward(
            current,
            gain_row,
            up_blocks,
            down_blocks,
            block_links,
            hidden_panels,
            model_panels,
            panel_width,
        )
        if moment < last_tick:
            arriving = from_behind(leaving, "pipe", 1)
    input_stack = jnp.stack(input_list)
    gain_total = jnp.zeros((model_width,), jnp.float32)
    grad_list = []
    normed_list = []
    upper_list = []
    active_list = []
    slope_list = []
    arriving = jnp.zeros((group_rows, model_width), jnp.bfloat16)
    for moment in range(last_tick + 1):
        slot_index = moment - (phases - 1 - section)
        slot_live = (slot_index >= 0) & (slot_index < MICRO)
        tick_place = jnp.clip(slot_index, 0, MICRO - 1) + section
        upstream = jnp.where(section == phases - 1, cot_groups_of[min(moment, MICRO - 1)], arriving)
        inputs = lax.dynamic_index_in_dim(input_stack, tick_place, 0, keepdims=False)
        before = up_product(inputs, gain_row, up_blocks, block_links, hidden_panels, panel_width)
        grad_local, gain_grad, normed, active, grad_before, upper = layer_backward(
            inputs,
            upstream,
            before,
            gain_row,
            up_blocks,
            down_blocks,
            block_links,
            hidden_panels,
            model_panels,
            panel_width,
        )
        gain_total = gain_total + jnp.where(slot_live, gain_grad, 0.0)
        grad_list.append(grad_local)
        normed_list.append(normed)
        upper_list.append(upper)
        active_list.append(active)
        slope_list.append(grad_before)
        if moment < last_tick:
            arriving = from_behind(grad_local, "pipe", -1)
    first = phases - 1 - section
    grad_store = own_slots(grad_list, first)
    normed_all = own_slots(normed_list, first)
    upper_all = own_slots(upper_list, first)
    active_all = own_slots(active_list, first)
    slope_all = own_slots(slope_list, first)
    grad_scale = 1.0 / math.sqrt(token_rows * lax.axis_size("dp"))
    up_total = jnp.einsum(
        "mbri,mbro->bio",
        jnp.take(normed_all, block_links[0], axis=1),
        jnp.take(slope_all, block_links[1], axis=1),
        preferred_element_type=jnp.float32,
    )
    down_total = jnp.einsum(
        "mbri,mbro->bio",
        jnp.take(active_all, block_links[2], axis=1),
        jnp.take(upper_all, block_links[3], axis=1),
        preferred_element_type=jnp.float32,
    )
    gain_parts = jnp.pad(
        gain_total.reshape(block_count, gain_count), ((0, 0), (0, 8 * 128 - gain_count))
    )
    totals = jnp.concatenate(
        [
            up_total.reshape(block_count, block_width),
            down_total.reshape(block_count, block_width),
            gain_parts,
        ],
        axis=1,
    )
    summed = lax.psum_scatter(
        totals.reshape(1, block_count, -1, 128), "dp", scatter_dimension=1, tiled=True
    ).reshape(-1) * grad_scale
    up_out = summed[:block_width].reshape(1, 1, panel_width, panel_width)
    down_out = summed[block_width : 2 * block_width].reshape(1, 1, panel_width, panel_width)
    gain_out = summed[2 * block_width : 2 * block_width + gain_count].reshape(1, gain_count)
    return (
        up_out,
        down_out,
        gain_out,
        grad_store.reshape(1, token_rows, model_width),
    )


def solution(mesh):
    in_specs = (
        P("dp", None),
        P("pipe", "dp"),
        P("pipe", "dp", None, None),
        P("pipe", "dp", None, None),
        P("pipe", None, None),
        P("dp", None),
    )
    out_specs = (
        P("pipe", "dp", None, None),
        P("pipe", "dp", None, None),
        P("pipe", "dp"),
        P("pipe", "dp", None),
    )
    return jax.shard_map(shards, mesh=mesh, in_specs=in_specs, out_specs=out_specs, check_vma=False)
```

```python
import math

import jax
import jax.numpy as jnp
from jax import lax
from jax.sharding import PartitionSpec as P

FF = 10240
MICRO = 2


epsilon = 1e-05


def from_behind(value, axis, by):
    size = lax.axis_size(axis)
    pairs = [(i, i + by) for i in range(size) if 0 <= i + by < size]
    return lax.ppermute(value, axis, pairs)


def norm_parts(inputs, gain_row):
    widened = inputs.astype(jnp.float32)
    inverse = lax.rsqrt(jnp.mean(widened * widened, axis=-1, keepdims=True) + epsilon)
    unit_rows = widened * inverse
    normed = (unit_rows * gain_row.astype(jnp.float32)).astype(jnp.bfloat16)
    return (widened, inverse, unit_rows, normed)


def to_panels(values, panel_width):
    row_count = values.shape[0]
    return jnp.transpose(values.reshape(row_count, -1, panel_width), (1, 0, 2))


def from_panels(panels):
    return jnp.transpose(panels, (1, 0, 2)).reshape(
        panels.shape[1], panels.shape[0] * panels.shape[2]
    )


def panel_product(panels, blocks, pick_index, put_index, put_count, form):
    picked = jnp.take(panels, pick_index, axis=0)
    products = jnp.einsum(form, picked, blocks, preferred_element_type=jnp.float32)
    placing = (put_index[:, None] == jnp.arange(put_count, dtype=jnp.int32)[None, :]).astype(
        jnp.float32
    )
    return jnp.einsum("brc,bp->prc", products, placing, precision=lax.Precision.HIGH)


def up_product(inputs, gain_row, up_blocks, block_links, hidden_panels, panel_width):
    normed = norm_parts(inputs, gain_row)[3]
    return panel_product(
        to_panels(normed, panel_width),
        up_blocks,
        block_links[0],
        block_links[1],
        hidden_panels,
        "bri,bio->bro",
    )


def layer_forward(
    inputs, gain_row, up_blocks, down_blocks, block_links, hidden_panels, model_panels, panel_width
):
    widened, inverse, unit_rows, normed = norm_parts(inputs, gain_row)
    before = panel_product(
        to_panels(normed, panel_width),
        up_blocks,
        block_links[0],
        block_links[1],
        hidden_panels,
        "bri,bio->bro",
    )
    active = jax.nn.gelu(before).astype(jnp.bfloat16)
    added = from_panels(
        panel_product(
            active, down_blocks, block_links[2], block_links[3], model_panels, "bri,bio->bro"
        )
    )
    return ((widened + added).astype(jnp.bfloat16), before)


def layer_backward(
    inputs,
    upstream,
    before,
    gain_row,
    up_blocks,
    down_blocks,
    block_links,
    hidden_panels,
    model_panels,
    panel_width,
):
    widened, inverse, unit_rows, normed = norm_parts(inputs, gain_row)
    upstream_panels = to_panels(upstream, panel_width)
    active_full, gelu_slope = jax.jvp(jax.nn.gelu, (before,), (jnp.ones_like(before),))
    active = active_full.astype(jnp.bfloat16)
    grad_active = panel_product(
        upstream_panels, down_blocks, block_links[3], block_links[2], hidden_panels, "bro,bio->bri"
    )
    grad_before = (grad_active * gelu_slope).astype(jnp.bfloat16)
    grad_normed = from_panels(
        panel_product(
            grad_before, up_blocks, block_links[1], block_links[0], model_panels, "bro,bio->bri"
        )
    )
    gain_grad = jnp.sum(grad_normed * unit_rows, axis=0)
    grad_unit = grad_normed * gain_row.astype(jnp.float32)
    centered = grad_unit - unit_rows * jnp.mean(grad_unit * unit_rows, axis=-1, keepdims=True)
    grad_local = (upstream.astype(jnp.float32) + inverse * centered).astype(jnp.bfloat16)
    return (
        grad_local,
        gain_grad,
        to_panels(normed, panel_width),
        active,
        grad_before,
        upstream_panels,
    )


def own_slots(collected, first):
    stacked = jnp.stack(collected)
    return lax.dynamic_slice_in_dim(stacked, first, MICRO, 0)


def shards(tokens, norm_gains, up_weights, down_weights, coords, cotangent):
    phases = lax.axis_size("pipe")
    section = lax.axis_index("pipe")
    panel_width = up_weights.shape[2]
    model_width = tokens.shape[1]
    token_rows = tokens.shape[0]
    hidden_panels = FF // panel_width
    model_panels = model_width // panel_width
    group_rows = token_rows // MICRO
    block_links = coords[0]
    block_width = panel_width * panel_width
    gain_count = norm_gains.shape[1]
    gain_room = -(-gain_count // 128) * 128
    packed = jnp.concatenate(
        [
            up_weights.reshape(1, 1, block_width),
            down_weights.reshape(1, 1, block_width),
            jnp.pad(norm_gains.reshape(1, 1, gain_count), ((0, 0), (0, 0), (0, gain_room - gain_count))),
        ],
        axis=2,
    )
    gathered = lax.all_gather(packed, "dp", axis=1, tiled=True)[0]
    block_count = gathered.shape[0]
    up_blocks = gathered[:, :block_width].reshape(block_count, panel_width, panel_width)
    down_blocks = gathered[:, block_width : 2 * block_width].reshape(
        block_count, panel_width, panel_width
    )
    gain_row = gathered[:, 2 * block_width : 2 * block_width + gain_count].reshape(-1)
    token_groups = tokens.reshape(MICRO, group_rows, model_width)
    cot_groups = cot_groups_of = cotangent.reshape(MICRO, group_rows, model_width)
    last_tick = MICRO + phases - 2
    input_list = []
    before_list = []
    arriving = jnp.zeros((group_rows, model_width), jnp.bfloat16)
    for moment in range(last_tick + 1):
        current = jnp.where(section == 0, token_groups[min(moment, MICRO - 1)], arriving)
        input_list.append(current)
        leaving, before = layer_forward(
            current,
            gain_row,
            up_blocks,
            down_blocks,
            block_links,
            hidden_panels,
            model_panels,
            panel_width,
        )
        before_list.append(before)
        if moment < last_tick:
            arriving = from_behind(leaving, "pipe", 1)
    input_stack = jnp.stack(input_list)
    before_stack = jnp.stack(before_list)
    gain_total = jnp.zeros((model_width,), jnp.float32)
    grad_list = []
    normed_list = []
    upper_list = []
    active_list = []
    slope_list = []
    arriving = jnp.zeros((group_rows, model_width), jnp.bfloat16)
    for moment in range(last_tick + 1):
        slot_index = moment - (phases - 1 - section)
        slot_live = (slot_index >= 0) & (slot_index < MICRO)
        tick_place = jnp.clip(slot_index, 0, MICRO - 1) + section
        upstream = jnp.where(section == phases - 1, cot_groups_of[min(moment, MICRO - 1)], arriving)
        inputs = lax.dynamic_index_in_dim(input_stack, tick_place, 0, keepdims=False)
        before = lax.dynamic_index_in_dim(before_stack, tick_place, 0, keepdims=False)
        grad_local, gain_grad, normed, active, grad_before, upper = layer_backward(
            inputs,
            upstream,
            before,
            gain_row,
            up_blocks,
            down_blocks,
            block_links,
            hidden_panels,
            model_panels,
            panel_width,
        )
        gain_total = gain_total + jnp.where(slot_live, gain_grad, 0.0)
        grad_list.append(grad_local)
        normed_list.append(normed)
        upper_list.append(upper)
        active_list.append(active)
        slope_list.append(grad_before)
        if moment < last_tick:
            arriving = from_behind(grad_local, "pipe", -1)
    first = phases - 1 - section
    grad_store = own_slots(grad_list, first)
    normed_all = own_slots(normed_list, first)
    upper_all = own_slots(upper_list, first)
    active_all = own_slots(active_list, first)
    slope_all = own_slots(slope_list, first)
    grad_scale = 1.0 / math.sqrt(token_rows * lax.axis_size("dp"))
    up_total = jnp.einsum(
        "mbri,mbro->bio",
        jnp.take(normed_all, block_links[0], axis=1),
        jnp.take(slope_all, block_links[1], axis=1),
        preferred_element_type=jnp.float32,
    )
    down_total = jnp.einsum(
        "mbri,mbro->bio",
        jnp.take(active_all, block_links[2], axis=1),
        jnp.take(upper_all, block_links[3], axis=1),
        preferred_element_type=jnp.float32,
    )
    gain_parts = jnp.pad(
        gain_total.reshape(block_count, gain_count), ((0, 0), (0, 8 * 128 - gain_count))
    )
    totals = jnp.concatenate(
        [
            up_total.reshape(block_count, block_width),
            down_total.reshape(block_count, block_width),
            gain_parts,
        ],
        axis=1,
    )
    summed = lax.psum_scatter(
        totals.reshape(1, block_count, -1, 128), "dp", scatter_dimension=1, tiled=True
    ).reshape(-1) * grad_scale
    up_out = summed[:block_width].reshape(1, 1, panel_width, panel_width)
    down_out = summed[block_width : 2 * block_width].reshape(1, 1, panel_width, panel_width)
    gain_out = summed[2 * block_width : 2 * block_width + gain_count].reshape(1, gain_count)
    return (
        up_out,
        down_out,
        gain_out,
        grad_store.reshape(1, token_rows, model_width),
    )


def solution(mesh):
    in_specs = (
        P("dp", None),
        P("pipe", "dp"),
        P("pipe", "dp", None, None),
        P("pipe", "dp", None, None),
        P("pipe", None, None),
        P("dp", None),
    )
    out_specs = (
        P("pipe", "dp", None, None),
        P("pipe", "dp", None, None),
        P("pipe", "dp"),
        P("pipe", "dp", None),
    )
    return jax.shard_map(shards, mesh=mesh, in_specs=in_specs, out_specs=out_specs, check_vma=False)
```

```python
import functools
import math

import jax
import jax.numpy as jnp
from jax import lax
from jax.experimental import pallas as pl
from jax.experimental.pallas import tpu as pltpu
from jax.sharding import PartitionSpec as P

FF = 10240
MICRO = 2


epsilon = 1e-05


def from_behind(value, axis, by):
    size = lax.axis_size(axis)
    pairs = [(i, i + by) for i in range(size) if 0 <= i + by < size]
    return lax.ppermute(value, axis, pairs)


def norm_parts(inputs, gain_row):
    widened = inputs.astype(jnp.float32)
    inverse = lax.rsqrt(jnp.mean(widened * widened, axis=-1, keepdims=True) + epsilon)
    unit_rows = widened * inverse
    normed = (unit_rows * gain_row.astype(jnp.float32)).astype(jnp.bfloat16)
    return (widened, inverse, unit_rows, normed)


def to_panels(values, panel_width):
    row_count = values.shape[0]
    return jnp.transpose(values.reshape(row_count, -1, panel_width), (1, 0, 2))


def from_panels(panels):
    return jnp.transpose(panels, (1, 0, 2)).reshape(
        panels.shape[1], panels.shape[0] * panels.shape[2]
    )


def _panel_kernel(pick_ref, put_ref, panels_ref, blocks_ref, out_ref, *, transpose):
    out_ref[...] = jnp.zeros_like(out_ref)

    def body(b, carry):
        source = panels_ref[pick_ref[b]]
        weight = blocks_ref[b]
        if transpose:
            product = lax.dot_general(
                source, weight, (((1,), (1,)), ((), ())), preferred_element_type=jnp.float32
            )
        else:
            product = jnp.dot(source, weight, preferred_element_type=jnp.float32)
        target = put_ref[b]
        out_ref[target] = out_ref[target] + product
        return carry

    lax.fori_loop(0, blocks_ref.shape[0], body, 0, unroll=True)


def panel_kernel(panels, blocks, pick_index, put_index, put_count, transpose):
    panel_count, rows, width = panels.shape
    block_count = blocks.shape[0]
    spec = pltpu.PrefetchScalarGridSpec(
        num_scalar_prefetch=2,
        grid=(1,),
        in_specs=[
            pl.BlockSpec((panel_count, rows, width), lambda i, *_: (0, 0, 0)),
            pl.BlockSpec(blocks.shape, lambda i, *_: (0, 0, 0)),
        ],
        out_specs=pl.BlockSpec((put_count, rows, width), lambda i, *_: (0, 0, 0)),
    )
    cost = pl.CostEstimate(
        flops=2 * block_count * rows * width * width,
        transcendentals=0,
        bytes_accessed=panels.size * 2 + blocks.size * 2 + put_count * rows * width * 4,
    )
    return pl.pallas_call(
        functools.partial(_panel_kernel, transpose=transpose),
        grid_spec=spec,
        out_shape=jax.ShapeDtypeStruct((put_count, rows, width), jnp.float32),
        cost_estimate=cost,
    )(pick_index, put_index, panels, blocks)


def panel_product(panels, blocks, pick_index, put_index, put_count, form):
    return panel_kernel(panels, blocks, pick_index, put_index, put_count, form == "bro,bio->bri")


def up_product(inputs, gain_row, up_blocks, block_links, hidden_panels, panel_width):
    normed = norm_parts(inputs, gain_row)[3]
    return panel_product(
        to_panels(normed, panel_width),
        up_blocks,
        block_links[0],
        block_links[1],
        hidden_panels,
        "bri,bio->bro",
    )


def layer_forward(
    inputs, gain_row, up_blocks, down_blocks, block_links, hidden_panels, model_panels, panel_width
):
    widened, inverse, unit_rows, normed = norm_parts(inputs, gain_row)
    before = panel_product(
        to_panels(normed, panel_width),
        up_blocks,
        block_links[0],
        block_links[1],
        hidden_panels,
        "bri,bio->bro",
    )
    active = jax.nn.gelu(before).astype(jnp.bfloat16)
    added = from_panels(
        panel_product(
            active, down_blocks, block_links[2], block_links[3], model_panels, "bri,bio->bro"
        )
    )
    return ((widened + added).astype(jnp.bfloat16), before)


def layer_backward(
    inputs,
    upstream,
    before,
    gain_row,
    up_blocks,
    down_blocks,
    block_links,
    hidden_panels,
    model_panels,
    panel_width,
):
    widened, inverse, unit_rows, normed = norm_parts(inputs, gain_row)
    upstream_panels = to_panels(upstream, panel_width)
    active_full, gelu_slope = jax.jvp(jax.nn.gelu, (before,), (jnp.ones_like(before),))
    active = active_full.astype(jnp.bfloat16)
    grad_active = panel_product(
        upstream_panels, down_blocks, block_links[3], block_links[2], hidden_panels, "bro,bio->bri"
    )
    grad_before = (grad_active * gelu_slope).astype(jnp.bfloat16)
    grad_normed = from_panels(
        panel_product(
            grad_before, up_blocks, block_links[1], block_links[0], model_panels, "bro,bio->bri"
        )
    )
    gain_grad = jnp.sum(grad_normed * unit_rows, axis=0)
    grad_unit = grad_normed * gain_row.astype(jnp.float32)
    centered = grad_unit - unit_rows * jnp.mean(grad_unit * unit_rows, axis=-1, keepdims=True)
    grad_local = (upstream.astype(jnp.float32) + inverse * centered).astype(jnp.bfloat16)
    return (
        grad_local,
        gain_grad,
        to_panels(normed, panel_width),
        active,
        grad_before,
        upstream_panels,
    )


def own_slots(collected, first):
    stacked = jnp.stack(collected)
    return lax.dynamic_slice_in_dim(stacked, first, MICRO, 0)


def shards(tokens, norm_gains, up_weights, down_weights, coords, cotangent):
    phases = lax.axis_size("pipe")
    section = lax.axis_index("pipe")
    panel_width = up_weights.shape[2]
    model_width = tokens.shape[1]
    token_rows = tokens.shape[0]
    hidden_panels = FF // panel_width
    model_panels = model_width // panel_width
    group_rows = token_rows // MICRO
    block_links = coords[0]
    block_width = panel_width * panel_width
    gain_count = norm_gains.shape[1]
    gain_room = -(-gain_count // 128) * 128
    packed = jnp.concatenate(
        [
            up_weights.reshape(1, 1, block_width),
            down_weights.reshape(1, 1, block_width),
            jnp.pad(norm_gains.reshape(1, 1, gain_count), ((0, 0), (0, 0), (0, gain_room - gain_count))),
        ],
        axis=2,
    )
    gathered = lax.all_gather(packed, "dp", axis=1, tiled=True)[0]
    block_count = gathered.shape[0]
    up_blocks = gathered[:, :block_width].reshape(block_count, panel_width, panel_width)
    down_blocks = gathered[:, block_width : 2 * block_width].reshape(
        block_count, panel_width, panel_width
    )
    gain_row = gathered[:, 2 * block_width : 2 * block_width + gain_count].reshape(-1)
    token_groups = tokens.reshape(MICRO, group_rows, model_width)
    cot_groups = cot_groups_of = cotangent.reshape(MICRO, group_rows, model_width)
    last_tick = MICRO + phases - 2
    input_list = []
    before_list = []
    arriving = jnp.zeros((group_rows, model_width), jnp.bfloat16)
    for moment in range(last_tick + 1):
        current = jnp.where(section == 0, token_groups[min(moment, MICRO - 1)], arriving)
        input_list.append(current)
        leaving, before = layer_forward(
            current,
            gain_row,
            up_blocks,
            down_blocks,
            block_links,
            hidden_panels,
            model_panels,
            panel_width,
        )
        before_list.append(before)
        if moment < last_tick:
            arriving = from_behind(leaving, "pipe", 1)
    input_stack = jnp.stack(input_list)
    before_stack = jnp.stack(before_list)
    gain_total = jnp.zeros((model_width,), jnp.float32)
    grad_list = []
    normed_list = []
    upper_list = []
    active_list = []
    slope_list = []
    arriving = jnp.zeros((group_rows, model_width), jnp.bfloat16)
    for moment in range(last_tick + 1):
        slot_index = moment - (phases - 1 - section)
        slot_live = (slot_index >= 0) & (slot_index < MICRO)
        tick_place = jnp.clip(slot_index, 0, MICRO - 1) + section
        upstream = jnp.where(section == phases - 1, cot_groups_of[min(moment, MICRO - 1)], arriving)
        inputs = lax.dynamic_index_in_dim(input_stack, tick_place, 0, keepdims=False)
        before = lax.dynamic_index_in_dim(before_stack, tick_place, 0, keepdims=False)
        grad_local, gain_grad, normed, active, grad_before, upper = layer_backward(
            inputs,
            upstream,
            before,
            gain_row,
            up_blocks,
            down_blocks,
            block_links,
            hidden_panels,
            model_panels,
            panel_width,
        )
        gain_total = gain_total + jnp.where(slot_live, gain_grad, 0.0)
        grad_list.append(grad_local)
        normed_list.append(normed)
        upper_list.append(upper)
        active_list.append(active)
        slope_list.append(grad_before)
        if moment < last_tick:
            arriving = from_behind(grad_local, "pipe", -1)
    first = phases - 1 - section
    grad_store = own_slots(grad_list, first)
    normed_all = own_slots(normed_list, first)
    upper_all = own_slots(upper_list, first)
    active_all = own_slots(active_list, first)
    slope_all = own_slots(slope_list, first)
    grad_scale = 1.0 / math.sqrt(token_rows * lax.axis_size("dp"))
    up_total = jnp.einsum(
        "mbri,mbro->bio",
        jnp.take(normed_all, block_links[0], axis=1),
        jnp.take(slope_all, block_links[1], axis=1),
        preferred_element_type=jnp.float32,
    )
    down_total = jnp.einsum(
        "mbri,mbro->bio",
        jnp.take(active_all, block_links[2], axis=1),
        jnp.take(upper_all, block_links[3], axis=1),
        preferred_element_type=jnp.float32,
    )
    gain_parts = jnp.pad(
        gain_total.reshape(block_count, gain_count), ((0, 0), (0, 8 * 128 - gain_count))
    )
    totals = jnp.concatenate(
        [
            up_total.reshape(block_count, block_width),
            down_total.reshape(block_count, block_width),
            gain_parts,
        ],
        axis=1,
    )
    summed = lax.psum_scatter(
        totals.reshape(1, block_count, -1, 128), "dp", scatter_dimension=1, tiled=True
    ).reshape(-1) * grad_scale
    up_out = summed[:block_width].reshape(1, 1, panel_width, panel_width)
    down_out = summed[block_width : 2 * block_width].reshape(1, 1, panel_width, panel_width)
    gain_out = summed[2 * block_width : 2 * block_width + gain_count].reshape(1, gain_count)
    return (
        up_out,
        down_out,
        gain_out,
        grad_store.reshape(1, token_rows, model_width),
    )


def solution(mesh):
    in_specs = (
        P("dp", None),
        P("pipe", "dp"),
        P("pipe", "dp", None, None),
        P("pipe", "dp", None, None),
        P("pipe", None, None),
        P("dp", None),
    )
    out_specs = (
        P("pipe", "dp", None, None),
        P("pipe", "dp", None, None),
        P("pipe", "dp"),
        P("pipe", "dp", None),
    )
    return jax.shard_map(shards, mesh=mesh, in_specs=in_specs, out_specs=out_specs, check_vma=False)
```

```python
import functools
import math

import jax
import jax.numpy as jnp
from jax import lax
from jax.experimental import pallas as pl
from jax.experimental.pallas import tpu as pltpu
from jax.sharding import PartitionSpec as P

FF = 10240
MICRO = 2


epsilon = 1e-05


def from_behind(value, axis, by):
    size = lax.axis_size(axis)
    pairs = [(i, i + by) for i in range(size) if 0 <= i + by < size]
    return lax.ppermute(value, axis, pairs)


def norm_parts(inputs, gain_row):
    widened = inputs.astype(jnp.float32)
    inverse = lax.rsqrt(jnp.mean(widened * widened, axis=-1, keepdims=True) + epsilon)
    unit_rows = widened * inverse
    normed = (unit_rows * gain_row.astype(jnp.float32)).astype(jnp.bfloat16)
    return (widened, inverse, unit_rows, normed)


def to_panels(values, panel_width):
    row_count = values.shape[0]
    return jnp.transpose(values.reshape(row_count, -1, panel_width), (1, 0, 2))


def from_panels(panels):
    return jnp.transpose(panels, (1, 0, 2)).reshape(
        panels.shape[1], panels.shape[0] * panels.shape[2]
    )


def _panel_kernel(pick_ref, put_ref, panels_ref, blocks_ref, out_ref, *, transpose):
    out_ref[...] = jnp.zeros_like(out_ref)

    def body(b, carry):
        source = panels_ref[pick_ref[b]]
        weight = blocks_ref[b]
        if transpose:
            product = lax.dot_general(
                source, weight, (((1,), (1,)), ((), ())), preferred_element_type=jnp.float32
            )
        else:
            product = jnp.dot(source, weight, preferred_element_type=jnp.float32)
        target = put_ref[b]
        out_ref[target] = out_ref[target] + product
        return carry

    lax.fori_loop(0, blocks_ref.shape[0], body, 0, unroll=True)


def panel_kernel(panels, blocks, pick_index, put_index, put_count, transpose):
    panel_count, rows, width = panels.shape
    block_count = blocks.shape[0]
    spec = pltpu.PrefetchScalarGridSpec(
        num_scalar_prefetch=2,
        grid=(1,),
        in_specs=[
            pl.BlockSpec((panel_count, rows, width), lambda i, *_: (0, 0, 0)),
            pl.BlockSpec(blocks.shape, lambda i, *_: (0, 0, 0)),
        ],
        out_specs=pl.BlockSpec((put_count, rows, width), lambda i, *_: (0, 0, 0)),
    )
    cost = pl.CostEstimate(
        flops=2 * block_count * rows * width * width,
        transcendentals=0,
        bytes_accessed=panels.size * 2 + blocks.size * 2 + put_count * rows * width * 4,
    )
    return pl.pallas_call(
        functools.partial(_panel_kernel, transpose=transpose),
        grid_spec=spec,
        out_shape=jax.ShapeDtypeStruct((put_count, rows, width), jnp.float32),
        cost_estimate=cost,
    )(pick_index, put_index, panels, blocks)


def panel_product(panels, blocks, pick_index, put_index, put_count, form):
    return panel_kernel(panels, blocks, pick_index, put_index, put_count, form == "bro,bio->bri")


def up_product(inputs, gain_row, up_blocks, block_links, hidden_panels, panel_width):
    normed = norm_parts(inputs, gain_row)[3]
    return panel_product(
        to_panels(normed, panel_width),
        up_blocks,
        block_links[0],
        block_links[1],
        hidden_panels,
        "bri,bio->bro",
    )


def layer_forward(
    inputs, gain_row, up_blocks, down_blocks, block_links, hidden_panels, model_panels, panel_width
):
    widened, inverse, unit_rows, normed = norm_parts(inputs, gain_row)
    before = panel_product(
        to_panels(normed, panel_width),
        up_blocks,
        block_links[0],
        block_links[1],
        hidden_panels,
        "bri,bio->bro",
    )
    active = jax.nn.gelu(before).astype(jnp.bfloat16)
    added = from_panels(
        panel_product(
            active, down_blocks, block_links[2], block_links[3], model_panels, "bri,bio->bro"
        )
    )
    return ((widened + added).astype(jnp.bfloat16), before)


def layer_backward(
    inputs,
    upstream,
    before,
    gain_row,
    up_blocks,
    down_blocks,
    block_links,
    hidden_panels,
    model_panels,
    panel_width,
):
    widened, inverse, unit_rows, normed = norm_parts(inputs, gain_row)
    upstream_panels = to_panels(upstream, panel_width)
    active_full, gelu_slope = jax.jvp(jax.nn.gelu, (before,), (jnp.ones_like(before),))
    active = active_full.astype(jnp.bfloat16)
    grad_active = panel_product(
        upstream_panels, down_blocks, block_links[3], block_links[2], hidden_panels, "bro,bio->bri"
    )
    grad_before = (grad_active * gelu_slope).astype(jnp.bfloat16)
    grad_normed = from_panels(
        panel_product(
            grad_before, up_blocks, block_links[1], block_links[0], model_panels, "bro,bio->bri"
        )
    )
    gain_grad = jnp.sum(grad_normed * unit_rows, axis=0)
    grad_unit = grad_normed * gain_row.astype(jnp.float32)
    centered = grad_unit - unit_rows * jnp.mean(grad_unit * unit_rows, axis=-1, keepdims=True)
    grad_local = (upstream.astype(jnp.float32) + inverse * centered).astype(jnp.bfloat16)
    return (
        grad_local,
        gain_grad,
        to_panels(normed, panel_width),
        active,
        grad_before,
        upstream_panels,
    )


def own_slots(collected, first):
    stacked = jnp.stack(collected)
    return lax.dynamic_slice_in_dim(stacked, first, MICRO, 0)


def shards(tokens, norm_gains, up_weights, down_weights, coords, cotangent):
    phases = lax.axis_size("pipe")
    section = lax.axis_index("pipe")
    panel_width = up_weights.shape[2]
    model_width = tokens.shape[1]
    token_rows = tokens.shape[0]
    hidden_panels = FF // panel_width
    model_panels = model_width // panel_width
    group_rows = token_rows // MICRO
    block_links = coords[0]
    gain_count = norm_gains.shape[1]
    gain_rows = 16
    packed = jnp.concatenate(
        [
            up_weights,
            down_weights,
            jnp.pad(
                norm_gains.reshape(1, 1, 1, gain_count),
                ((0, 0), (0, 0), (0, gain_rows - 1), (0, panel_width - gain_count)),
            ),
        ],
        axis=2,
    )
    gathered = lax.all_gather(packed, "dp", axis=1, tiled=True)[0]
    block_count = gathered.shape[0]
    up_blocks = gathered[:, :panel_width]
    down_blocks = gathered[:, panel_width : 2 * panel_width]
    gain_row = gathered[:, 2 * panel_width, :gain_count].reshape(-1)
    token_groups = tokens.reshape(MICRO, group_rows, model_width)
    cot_groups = cot_groups_of = cotangent.reshape(MICRO, group_rows, model_width)
    last_tick = MICRO + phases - 2
    input_list = []
    before_list = []
    arriving = jnp.zeros((group_rows, model_width), jnp.bfloat16)
    for moment in range(last_tick + 1):
        current = jnp.where(section == 0, token_groups[min(moment, MICRO - 1)], arriving)
        input_list.append(current)
        leaving, before = layer_forward(
            current,
            gain_row,
            up_blocks,
            down_blocks,
            block_links,
            hidden_panels,
            model_panels,
            panel_width,
        )
        before_list.append(before)
        if moment < last_tick:
            arriving = from_behind(leaving, "pipe", 1)
    input_stack = jnp.stack(input_list)
    before_stack = jnp.stack(before_list)
    gain_total = jnp.zeros((model_width,), jnp.float32)
    grad_list = []
    normed_list = []
    upper_list = []
    active_list = []
    slope_list = []
    arriving = jnp.zeros((group_rows, model_width), jnp.bfloat16)
    for moment in range(last_tick + 1):
        slot_index = moment - (phases - 1 - section)
        slot_live = (slot_index >= 0) & (slot_index < MICRO)
        tick_place = jnp.clip(slot_index, 0, MICRO - 1) + section
        upstream = jnp.where(section == phases - 1, cot_groups_of[min(moment, MICRO - 1)], arriving)
        inputs = lax.dynamic_index_in_dim(input_stack, tick_place, 0, keepdims=False)
        before = lax.dynamic_index_in_dim(before_stack, tick_place, 0, keepdims=False)
        grad_local, gain_grad, normed, active, grad_before, upper = layer_backward(
            inputs,
            upstream,
            before,
            gain_row,
            up_blocks,
            down_blocks,
            block_links,
            hidden_panels,
            model_panels,
            panel_width,
        )
        gain_total = gain_total + jnp.where(slot_live, gain_grad, 0.0)
        grad_list.append(grad_local)
        normed_list.append(normed)
        upper_list.append(upper)
        active_list.append(active)
        slope_list.append(grad_before)
        if moment < last_tick:
            arriving = from_behind(grad_local, "pipe", -1)
    first = phases - 1 - section
    grad_store = own_slots(grad_list, first)
    normed_all = own_slots(normed_list, first)
    upper_all = own_slots(upper_list, first)
    active_all = own_slots(active_list, first)
    slope_all = own_slots(slope_list, first)
    grad_scale = 1.0 / math.sqrt(token_rows * lax.axis_size("dp"))
    up_total = jnp.einsum(
        "mbri,mbro->bio",
        jnp.take(normed_all, block_links[0], axis=1),
        jnp.take(slope_all, block_links[1], axis=1),
        preferred_element_type=jnp.float32,
    )
    down_total = jnp.einsum(
        "mbri,mbro->bio",
        jnp.take(active_all, block_links[2], axis=1),
        jnp.take(upper_all, block_links[3], axis=1),
        preferred_element_type=jnp.float32,
    )
    gain_parts = jnp.pad(
        gain_total.reshape(block_count, 1, gain_count),
        ((0, 0), (0, 7), (0, panel_width - gain_count)),
    )
    totals = jnp.concatenate([up_total, down_total, gain_parts], axis=1)
    summed = lax.psum_scatter(totals[None], "dp", scatter_dimension=1, tiled=True) * grad_scale
    up_out = summed[:, :, :panel_width]
    down_out = summed[:, :, panel_width : 2 * panel_width]
    gain_out = summed[0, :, 2 * panel_width, :gain_count]
    return (
        up_out,
        down_out,
        gain_out,
        grad_store.reshape(1, token_rows, model_width),
    )


def solution(mesh):
    in_specs = (
        P("dp", None),
        P("pipe", "dp"),
        P("pipe", "dp", None, None),
        P("pipe", "dp", None, None),
        P("pipe", None, None),
        P("dp", None),
    )
    out_specs = (
        P("pipe", "dp", None, None),
        P("pipe", "dp", None, None),
        P("pipe", "dp"),
        P("pipe", "dp", None),
    )
    return jax.shard_map(shards, mesh=mesh, in_specs=in_specs, out_specs=out_specs, check_vma=False)
```
